32 devices in a mesh: owner: 2 (over x), reader: 16 (over z, y, core).
Axes of the slice: x: 2, y: 2, z: 4, core: 2. Of those that a mesh axis runs over, the one named last changes fastest.
Arguments:
- acts: bfloat16 [256, 4096], P('reader', 'owner'), may hold values from -6 to 6
- grads: bfloat16 [256, 14336], P('reader', 'owner'), may hold values from -6 to 6
- basis_a: bfloat16 [4096, 4096], P('reader', 'owner'), may hold values from -0.09375 to 0.09375
- basis_g: bfloat16 [14336, 14336], P('reader', 'owner'), may hold values from -0.046875 to 0.046875
- eigvals: bfloat16 [14336, 4096], P('reader', 'owner'), may hold values from 0.099609375 to 10
- lengths: int32 [2], replicated, may hold values from 1 to 128, as said below
- shuffle: int32 [2], replicated, may hold values from 0 to 1, each once
Outputs:
- token_score: float32 [256], P('owner')
- example_score: float32 [2], replicated
The draws below stay inside these ranges and needn't reach their ends.
Inputs may be any that keep to these rules, and one draw needn't show every extreme that they name: `lengths`: some slot has exactly 128 live tokens. `shuffle`: each example id appears once.
All inputs are finite; a program needn't handle non-finite values.
Results may differ from the reference program's by a relative error of at most 0.0003.
Values may be sent and summed in bfloat16 or wider, within the bound.
No kernel may reach another device: no remote copies, remote signals or barrier semaphores. Data moves between devices by JAX's collectives and lax.ppermute only.
A program may use at most 128 MiB of HBM per device.

```python
import math
import jax
import jax.numpy as jnp
from jax import lax

D = 4096
FF = 14336
SEQ = 128
EXAMPLES = 2
TOKENS = 256


def draw_lengths(key, part):
    first_key = jax.random.fold_in(key, 11)
    second_key = jax.random.fold_in(key, 23)
    values = jax.random.randint(first_key, (EXAMPLES,), 1, SEQ + 1, dtype=jnp.int32)
    full_slot = jax.random.randint(second_key, (), 0, EXAMPLES, dtype=jnp.int32)
    slot_ids = jnp.arange(EXAMPLES, dtype=jnp.int32)
    return jnp.where(slot_ids == full_slot, jnp.int32(SEQ), values).astype(jnp.int32)


def steps_of(key, dims, cuts, smallest, largest):
    loudness = 1.0
    for dim, blocks in cuts:
        draws = jax.random.uniform(jax.random.fold_in(jax.random.fold_in(key, 6), dim), (blocks,), jnp.float32, smallest / len(cuts), largest / len(cuts))
        loudness = loudness * jnp.repeat(jnp.exp(draws), dims[dim] // blocks).reshape((-1,) + (1,) * (len(dims) - 1 - dim))
    return loudness


def bell_draw(stream_key, dims, spread, most, shards=(), held_as=jnp.bfloat16):
    drawn = spread * jax.random.normal(stream_key, dims, jnp.float32)
    if shards:
        drawn = drawn * steps_of(stream_key, dims, shards, -0.22, 0.18)
    return jnp.clip(drawn, -most, most).astype(held_as)


def setup_inputs(seed: int = 0) -> dict:
    key_of = jax.random.split(jax.random.key(seed), 8)
    return {
        "acts": bell_draw(key_of[0], (TOKENS, D), 1.0, 6.0, ((0, 16), (1, 2))),
        "grads": bell_draw(key_of[1], (TOKENS, FF), 1.0, 6.0, ((0, 16), (1, 2))),
        "basis_a": bell_draw(key_of[2], (D, D), D ** -0.5, 0.09375, ((0, 16), (1, 2))),
        "basis_g": bell_draw(key_of[3], (FF, FF), FF ** -0.5, 0.046875, ((0, 16), (1, 2))),
        "eigvals": jnp.clip(jnp.exp(math.log(10.0) - 4.609084 * jax.random.uniform(key_of[4], (FF, D), jnp.float32) ** steps_of(key_of[4], (FF, D), ((0, 16), (1, 2)), -0.2, 0.2)), 0.099609375, 10.0).astype(jnp.bfloat16),
        "lengths": draw_lengths(jax.random.fold_in(key_of[7], 71), 0),
        "shuffle": jax.random.permutation(key_of[6], EXAMPLES).astype(jnp.int32),
    }


def reference(acts, grads, basis_a, basis_g, eigvals, lengths, shuffle):
    slots = jnp.arange(TOKENS, dtype=jnp.int32)
    live = ((slots % SEQ) < lengths[slots // SEQ]).astype(jnp.float32)
    rot_a = (jnp.dot(acts, basis_a.T, preferred_element_type=jnp.float32) * live[:, None]).astype(jnp.bfloat16)
    rot_g = (jnp.dot(grads, basis_g.T, preferred_element_type=jnp.float32) * live[:, None]).astype(jnp.bfloat16)
    denom = eigvals.astype(jnp.float32)

    def one_slot(index):
        start = (index * SEQ).astype(jnp.int32)
        g_rows = lax.dynamic_slice_in_dim(rot_g, start, SEQ, 0)
        a_rows = lax.dynamic_slice_in_dim(rot_a, start, SEQ, 0)
        outer = jnp.dot(g_rows.T, a_rows, preferred_element_type=jnp.float32)
        scaled = (outer / denom).astype(jnp.bfloat16)
        projected = jnp.dot(g_rows, scaled, preferred_element_type=jnp.float32)
        return jnp.sum(projected * a_rows.astype(jnp.float32), axis=1) / (FF * D)

    scores = lax.map(one_slot, jnp.arange(EXAMPLES, dtype=jnp.int32))
    token_score = scores.reshape(TOKENS)
    slot_mean = jnp.sum(scores, axis=1) / SEQ
    example_score = jnp.zeros((EXAMPLES,), jnp.float32).at[shuffle].set(slot_mean)
    return token_score, example_score
```

```python
import jax
import jax.numpy as jnp
from jax import lax
from jax.sharding import PartitionSpec as P

SEQ = 128


def local(acts, grads, basis_a, basis_g, eigvals, lengths, shuffle):
    owners = lax.axis_size("owner")
    readers = lax.axis_size("reader")
    owner_index = lax.axis_index("owner")
    rows = acts.shape[0] * readers
    slots = rows // SEQ
    m_block = basis_g.shape[0]
    n_block = basis_a.shape[0]
    width = eigvals.shape[1]
    dim_ff = m_block * readers
    dim_d = width * owners

    joined = jnp.concatenate([grads, acts], axis=1)
    joined = lax.all_gather(joined, "reader", axis=0, tiled=True)
    all_g = joined[:, : grads.shape[1]]
    all_a = joined[:, grads.shape[1]:]

    part_g = jnp.einsum("tk,jk->tj", all_g, basis_g, preferred_element_type=jnp.float32)
    part_a = jnp.einsum("tk,jk->tj", all_a, basis_a, preferred_element_type=jnp.float32)
    part = jnp.concatenate([part_g, part_a], axis=1)
    whole = lax.psum(part, "owner")

    token = jnp.arange(rows, dtype=jnp.int32)
    live = ((token % SEQ) < lengths[token // SEQ]).astype(jnp.float32)
    rot = (whole * live[:, None]).astype(jnp.bfloat16)
    rot_g = rot[:, :m_block]
    rot_a_block = rot[:, m_block:]

    rot_a_all = lax.all_gather(rot_a_block, "reader", axis=1, tiled=True)
    rot_a = lax.dynamic_slice_in_dim(rot_a_all, owner_index * width, width, axis=1)

    denom = eigvals.astype(jnp.float32)
    g_rows = rot_g.reshape(slots, SEQ, m_block)
    a_rows = rot_a.reshape(slots, SEQ, width)
    outer = jnp.einsum("smt,smn->stn", g_rows, a_rows, preferred_element_type=jnp.float32)
    scaled = (outer / denom[None]).astype(jnp.bfloat16)
    projected = jnp.einsum("stm,smn->stn", g_rows, scaled, preferred_element_type=jnp.float32)
    partial = jnp.sum(projected * a_rows.astype(jnp.float32), axis=2) / (dim_ff * dim_d)
    scores = lax.psum(partial, ("owner", "reader"))

    token_score = lax.dynamic_index_in_dim(scores, owner_index, 0, keepdims=False)
    slot_mean = jnp.sum(scores, axis=1) / SEQ
    table = (shuffle[:, None] == jnp.arange(slots, dtype=jnp.int32)[None, :]).astype(jnp.float32)
    example_score = jnp.sum(slot_mean[:, None] * table, axis=0)
    return (token_score, example_score)


def solution(mesh):
    return jax.shard_map(
        local,
        mesh=mesh,
        in_specs=(
            P("reader", "owner"),
            P("reader", "owner"),
            P("reader", "owner"),
            P("reader", "owner"),
            P("reader", "owner"),
            P(),
            P(),
        ),
        out_specs=(P("owner"), P()),
        check_vma=False,
    )
```

```python
import jax
import jax.numpy as jnp
from jax import lax
from jax.sharding import PartitionSpec as P

SEQ = 128


def butterfly_sum(x, axis, size):
    if size & (size - 1):
        return lax.psum(x, axis)
    bit = 1
    while bit < size:
        x = x + lax.ppermute(x, axis, [(i, i ^ bit) for i in range(size)])
        bit *= 2
    return x


def local(acts, grads, basis_a, basis_g, eigvals, lengths, shuffle):
    owners = lax.axis_size("owner")
    readers = lax.axis_size("reader")
    owner_index = lax.axis_index("owner")
    rows = acts.shape[0] * readers
    slots = rows // SEQ
    m_block = basis_g.shape[0]
    n_block = basis_a.shape[0]
    width = eigvals.shape[1]
    dim_ff = m_block * readers
    dim_d = width * owners

    joined = jnp.concatenate([grads, acts], axis=1)
    joined = lax.all_gather(joined, "reader", axis=0, tiled=True)
    all_g = joined[:, : grads.shape[1]]
    all_a = joined[:, grads.shape[1]:]

    token = jnp.arange(rows, dtype=jnp.int32)
    live = ((token % SEQ) < lengths[token // SEQ]).astype(jnp.float32)

    part_a = jnp.einsum("tk,jk->tj", all_a, basis_a, preferred_element_type=jnp.float32)
    rot_a_block = (butterfly_sum(part_a, "owner", owners) * live[:, None]).astype(jnp.bfloat16)
    part_g = jnp.einsum("tk,jk->tj", all_g, basis_g, preferred_element_type=jnp.float32)
    rot_g = (butterfly_sum(part_g, "owner", owners) * live[:, None]).astype(jnp.bfloat16)

    rot_a_all = lax.all_gather(rot_a_block, "reader", axis=1, tiled=True)
    rot_a = lax.dynamic_slice_in_dim(rot_a_all, owner_index * width, width, axis=1)

    denom = eigvals.astype(jnp.float32)
    g_rows = rot_g.reshape(slots, SEQ, m_block)
    a_rows = rot_a.reshape(slots, SEQ, width)
    outer = jnp.einsum("smt,smn->stn", g_rows, a_rows, preferred_element_type=jnp.float32)
    scaled = (outer / denom[None]).astype(jnp.bfloat16)
    projected = jnp.einsum("stm,smn->stn", g_rows, scaled, preferred_element_type=jnp.float32)
    partial = jnp.sum(projected * a_rows.astype(jnp.float32), axis=2) / (dim_ff * dim_d)
    scores = butterfly_sum(butterfly_sum(partial, "reader", readers), "owner", owners)

    token_score = lax.dynamic_index_in_dim(scores, owner_index, 0, keepdims=False)
    slot_mean = jnp.sum(scores, axis=1) / SEQ
    table = (shuffle[:, None] == jnp.arange(slots, dtype=jnp.int32)[None, :]).astype(jnp.float32)
    example_score = jnp.sum(slot_mean[:, None] * table, axis=0)
    return (token_score, example_score)


def solution(mesh):
    return jax.shard_map(
        local,
        mesh=mesh,
        in_specs=(
            P("reader", "owner"),
            P("reader", "owner"),
            P("reader", "owner"),
            P("reader", "owner"),
            P("reader", "owner"),
            P(),
            P(),
        ),
        out_specs=(P("owner"), P()),
        check_vma=False,
    )
```

```python
import jax
import jax.numpy as jnp
from jax import lax
from jax.sharding import PartitionSpec as P

SEQ = 128


def butterfly_sum(x, axis, size):
    if size & (size - 1):
        return lax.psum(x, axis)
    bit = 1
    while bit < size:
        x = x + lax.ppermute(x, axis, [(i, i ^ bit) for i in range(size)])
        bit *= 2
    return x


def half_gather(block, owners, readers):
    reader_index = lax.axis_index("reader")
    owner_index = lax.axis_index("owner")
    group = readers // owners
    held = block
    bit = readers // 2
    while bit >= group:
        other = lax.ppermute(held, "reader", [(i, i ^ bit) for i in range(readers)])
        keep = (reader_index & bit) == ((owner_index * group) & bit)
        held = jnp.where(keep, held, other)
        bit //= 2
    held = held[None]
    while bit >= 1:
        other = lax.ppermute(held, "reader", [(i, i ^ bit) for i in range(readers)])
        low = (reader_index & bit) == 0
        first = jnp.where(low, held, other)
        second = jnp.where(low, other, held)
        held = jnp.stack([first, second], axis=1).reshape((-1,) + block.shape)
        bit //= 2
    return jnp.transpose(held, (1, 0, 2)).reshape(block.shape[0], -1)


def local(acts, grads, basis_a, basis_g, eigvals, lengths, shuffle):
    owners = lax.axis_size("owner")
    readers = lax.axis_size("reader")
    owner_index = lax.axis_index("owner")
    rows = acts.shape[0] * readers
    slots = rows // SEQ
    m_block = basis_g.shape[0]
    n_block = basis_a.shape[0]
    width = eigvals.shape[1]
    dim_ff = m_block * readers
    dim_d = width * owners

    joined = jnp.concatenate([grads, acts], axis=1)
    joined = lax.all_gather(joined, "reader", axis=0, tiled=True)
    all_g = joined[:, : grads.shape[1]]
    all_a = joined[:, grads.shape[1]:]

    token = jnp.arange(rows, dtype=jnp.int32)
    live = ((token % SEQ) < lengths[token // SEQ]).astype(jnp.float32)

    part_a = jnp.einsum("tk,jk->tj", all_a, basis_a, preferred_element_type=jnp.float32)
    rot_a_block = (butterfly_sum(part_a, "owner", owners) * live[:, None]).astype(jnp.bfloat16)
    part_g = jnp.einsum("tk,jk->tj", all_g, basis_g, preferred_element_type=jnp.float32)
    rot_g = (butterfly_sum(part_g, "owner", owners) * live[:, None]).astype(jnp.bfloat16)

    rot_a = half_gather(rot_a_block, owners, readers)

    denom = eigvals.astype(jnp.float32)
    g_rows = rot_g.reshape(slots, SEQ, m_block)
    a_rows = rot_a.reshape(slots, SEQ, width)
    outer = jnp.einsum("smt,smn->stn", g_rows, a_rows, preferred_element_type=jnp.float32)
    scaled = (outer / denom[None]).astype(jnp.bfloat16)
    projected = jnp.einsum("stm,smn->stn", g_rows, scaled, preferred_element_type=jnp.float32)
    partial = jnp.sum(projected * a_rows.astype(jnp.float32), axis=2) / (dim_ff * dim_d)
    scores = butterfly_sum(butterfly_sum(partial, "reader", readers), "owner", owners)

    token_score = lax.dynamic_index_in_dim(scores, owner_index, 0, keepdims=False)
    slot_mean = jnp.sum(scores, axis=1) / SEQ
    table = (shuffle[:, None] == jnp.arange(slots, dtype=jnp.int32)[None, :]).astype(jnp.float32)
    example_score = jnp.sum(slot_mean[:, None] * table, axis=0)
    return (token_score, example_score)


def solution(mesh):
    return jax.shard_map(
        local,
        mesh=mesh,
        in_specs=(
            P("reader", "owner"),
            P("reader", "owner"),
            P("reader", "owner"),
            P("reader", "owner"),
            P("reader", "owner"),
            P(),
            P(),
        ),
        out_specs=(P("owner"), P()),
        check_vma=False,
    )
```

```python
import jax
import jax.numpy as jnp
from jax import lax
from jax.sharding import PartitionSpec as P

SEQ = 128


def bit_groups(bits):
    return [bits[i:i + 2] for i in range(0, len(bits), 2)]


def xor_round(held, axis, size, group):
    parts = [held]
    for count in range(1, 1 << len(group)):
        c = sum(bit for k, bit in enumerate(group) if count >> k & 1)
        parts.append(lax.ppermute(held, axis, [(i, i ^ c) for i in range(size)]))
    return jnp.stack(parts)


def counter_of(c, group):
    out = jnp.zeros_like(c)
    for k, bit in enumerate(group):
        out = out + (((c >> (bit.bit_length() - 1)) & 1) << k)
    return out


def xor_sum(x, axis, size):
    if size & (size - 1):
        return lax.psum(x, axis)
    index = lax.axis_index(axis)
    bits = [1 << k for k in range(size.bit_length() - 1)][::-1]
    for group in bit_groups(bits):
        mask = sum(group)
        stacked = xor_round(x, axis, size, group)
        order = [counter_of((v ^ (index & mask)), group) for v in range(mask + 1) if v & ~mask == 0]
        terms = [stacked[k] for k in order]
        while len(terms) > 1:
            terms = [terms[i] + terms[i + 1] for i in range(0, len(terms), 2)]
        x = terms[0]
    return x


def half_gather(block, owners, readers):
    reader_index = lax.axis_index("reader")
    owner_index = lax.axis_index("owner")
    group_size = readers // owners
    bits = [1 << k for k in range(readers.bit_length() - 1)][::-1]
    target = owner_index * group_size
    held = block[None]
    for group in bit_groups(bits):
        high = sum(bit for bit in group if bit >= group_size)
        low = [bit for bit in group if bit < group_size]
        stacked = xor_round(held, "reader", readers, group)
        c_high = (reader_index ^ target) & high
        picks = []
        values = sorted(sum(bit for k, bit in enumerate(low) if count >> k & 1) for count in range(1 << len(low)))
        for v in values:
            c = c_high + (v ^ (reader_index & sum(low)))
            picks.append(counter_of(c, group))
        chosen = jnp.take(stacked, jnp.stack(picks), axis=0)
        chosen = jnp.swapaxes(chosen, 0, 1)
        held = chosen.reshape((-1,) + block.shape)
    return jnp.transpose(held, (1, 0, 2)).reshape(block.shape[0], -1)


def local(acts, grads, basis_a, basis_g, eigvals, lengths, shuffle):
    owners = lax.axis_size("owner")
    readers = lax.axis_size("reader")
    owner_index = lax.axis_index("owner")
    rows = acts.shape[0] * readers
    slots = rows // SEQ
    m_block = basis_g.shape[0]
    n_block = basis_a.shape[0]
    width = eigvals.shape[1]
    dim_ff = m_block * readers
    dim_d = width * owners

    joined = jnp.concatenate([grads, acts], axis=1)
    joined = lax.all_gather(joined, "reader", axis=0, tiled=True)
    all_g = joined[:, : grads.shape[1]]
    all_a = joined[:, grads.shape[1]:]

    token = jnp.arange(rows, dtype=jnp.int32)
    live = ((token % SEQ) < lengths[token // SEQ]).astype(jnp.float32)

    part_a = jnp.einsum("tk,jk->tj", all_a, basis_a, preferred_element_type=jnp.float32)
    rot_a_block = (xor_sum(part_a, "owner", owners) * live[:, None]).astype(jnp.bfloat16)
    part_g = jnp.einsum("tk,jk->tj", all_g, basis_g, preferred_element_type=jnp.float32)
    rot_g = (xor_sum(part_g, "owner", owners) * live[:, None]).astype(jnp.bfloat16)

    rot_a = half_gather(rot_a_block, owners, readers)

    denom = eigvals.astype(jnp.float32)
    g_rows = rot_g.reshape(slots, SEQ, m_block)
    a_rows = rot_a.reshape(slots, SEQ, width)
    outer = jnp.einsum("smt,smn->stn", g_rows, a_rows, preferred_element_type=jnp.float32)
    scaled = (outer / denom[None]).astype(jnp.bfloat16)
    projected = jnp.einsum("stm,smn->stn", g_rows, scaled, preferred_element_type=jnp.float32)
    partial = jnp.sum(projected * a_rows.astype(jnp.float32), axis=2) / (dim_ff * dim_d)
    scores = xor_sum(xor_sum(partial, "reader", readers), "owner", owners)

    token_score = lax.dynamic_index_in_dim(scores, owner_index, 0, keepdims=False)
    slot_mean = jnp.sum(scores, axis=1) / SEQ
    table = (shuffle[:, None] == jnp.arange(slots, dtype=jnp.int32)[None, :]).astype(jnp.float32)
    example_score = jnp.sum(slot_mean[:, None] * table, axis=0)
    return (token_score, example_score)


def solution(mesh):
    return jax.shard_map(
        local,
        mesh=mesh,
        in_specs=(
            P("reader", "owner"),
            P("reader", "owner"),
            P("reader", "owner"),
            P("reader", "owner"),
            P("reader", "owner"),
            P(),
            P(),
        ),
        out_specs=(P("owner"), P()),
        check_vma=False,
    )
```

```python
import jax
import jax.numpy as jnp
from jax import lax
from jax.sharding import PartitionSpec as P

SEQ = 128


def bit_groups(bits):
    return [bits[i:i + 2] for i in range(0, len(bits), 2)]


def xor_round(held, axis, size, group):
    parts = [held]
    for count in range(1, 1 << len(group)):
        c = sum(bit for k, bit in enumerate(group) if count >> k & 1)
        parts.append(lax.ppermute(held, axis, [(i, i ^ c) for i in range(size)]))
    return jnp.stack(parts)


def counter_of(c, group):
    out = jnp.zeros_like(c)
    for k, bit in enumerate(group):
        out = out + (((c >> (bit.bit_length() - 1)) & 1) << k)
    return out


def xor_sum(x, axis, size):
    if size & (size - 1):
        return lax.psum(x, axis)
    index = lax.axis_index(axis)
    bits = [1 << k for k in range(size.bit_length() - 1)][::-1]
    for group in bit_groups(bits):
        mask = sum(group)
        stacked = xor_round(x, axis, size, group)
        order = [counter_of((v ^ (index & mask)), group) for v in range(mask + 1) if v & ~mask == 0]
        terms = [stacked[k] for k in order]
        while len(terms) > 1:
            terms = [terms[i] + terms[i + 1] for i in range(0, len(terms), 2)]
        x = terms[0]
    return x


def ordered_gather(block, owners, readers):
    reader_index = lax.axis_index("reader")
    owner_index = lax.axis_index("owner") if owners > 1 else 0
    group_size = readers // owners
    bits = [1 << k for k in range(readers.bit_length() - 1)][::-1]
    target = owner_index * group_size
    held = block[None]
    for group in bit_groups(bits):
        high = sum(bit for bit in group if bit >= group_size)
        low = [bit for bit in group if bit < group_size]
        stacked = xor_round(held, "reader", readers, group)
        c_high = (reader_index ^ target) & high
        picks = []
        values = sorted(sum(bit for k, bit in enumerate(low) if count >> k & 1) for count in range(1 << len(low)))
        for v in values:
            c = c_high + (v ^ (reader_index & sum(low)))
            picks.append(counter_of(c, group))
        chosen = jnp.take(stacked, jnp.stack(picks), axis=0)
        chosen = jnp.swapaxes(chosen, 0, 1)
        held = chosen.reshape((-1,) + block.shape)
    return held


def half_gather(block, owners, readers):
    held = ordered_gather(block, owners, readers)
    return jnp.transpose(held, (1, 0, 2)).reshape(block.shape[0], -1)


def local(acts, grads, basis_a, basis_g, eigvals, lengths, shuffle):
    owners = lax.axis_size("owner")
    readers = lax.axis_size("reader")
    owner_index = lax.axis_index("owner")
    rows = acts.shape[0] * readers
    slots = rows // SEQ
    m_block = basis_g.shape[0]
    n_block = basis_a.shape[0]
    width = eigvals.shape[1]
    dim_ff = m_block * readers
    dim_d = width * owners

    all_g = lax.all_gather(grads, "reader", axis=0, tiled=True)
    all_a = ordered_gather(acts, 1, readers).reshape(rows, acts.shape[1])

    token = jnp.arange(rows, dtype=jnp.int32)
    live = ((token % SEQ) < lengths[token // SEQ]).astype(jnp.float32)

    part_a = jnp.einsum("tk,jk->tj", all_a, basis_a, preferred_element_type=jnp.float32)
    rot_a_block = (xor_sum(part_a, "owner", owners) * live[:, None]).astype(jnp.bfloat16)
    part_g = jnp.einsum("tk,jk->tj", all_g, basis_g, preferred_element_type=jnp.float32)
    rot_g = (xor_sum(part_g, "owner", owners) * live[:, None]).astype(jnp.bfloat16)

    rot_a = half_gather(rot_a_block, owners, readers)

    denom = eigvals.astype(jnp.float32)
    g_rows = rot_g.reshape(slots, SEQ, m_block)
    a_rows = rot_a.reshape(slots, SEQ, width)
    outer = jnp.einsum("smt,smn->stn", g_rows, a_rows, preferred_element_type=jnp.float32)
    scaled = (outer / denom[None]).astype(jnp.bfloat16)
    projected = jnp.einsum("stm,smn->stn", g_rows, scaled, preferred_element_type=jnp.float32)
    partial = jnp.sum(projected * a_rows.astype(jnp.float32), axis=2) / (dim_ff * dim_d)
    scores = xor_sum(xor_sum(partial, "reader", readers), "owner", owners)

    token_score = lax.dynamic_index_in_dim(scores, owner_index, 0, keepdims=False)
    slot_mean = jnp.sum(scores, axis=1) / SEQ
    table = (shuffle[:, None] == jnp.arange(slots, dtype=jnp.int32)[None, :]).astype(jnp.float32)
    example_score = jnp.sum(slot_mean[:, None] * table, axis=0)
    return (token_score, example_score)


def solution(mesh):
    return jax.shard_map(
        local,
        mesh=mesh,
        in_specs=(
            P("reader", "owner"),
            P("reader", "owner"),
            P("reader", "owner"),
            P("reader", "owner"),
            P("reader", "owner"),
            P(),
            P(),
        ),
        out_specs=(P("owner"), P()),
        check_vma=False,
    )
```

```python
import jax
import jax.numpy as jnp
from jax import lax
from jax.sharding import PartitionSpec as P

SEQ = 128


def bit_groups(bits):
    return [bits[i:i + 2] for i in range(0, len(bits), 2)]


def xor_round(held, axis, size, group):
    parts = [held]
    for count in range(1, 1 << len(group)):
        c = sum(bit for k, bit in enumerate(group) if count >> k & 1)
        parts.append(lax.ppermute(held, axis, [(i, i ^ c) for i in range(size)]))
    return jnp.stack(parts)


def counter_of(c, group):
    out = jnp.zeros_like(c)
    for k, bit in enumerate(group):
        out = out + (((c >> (bit.bit_length() - 1)) & 1) << k)
    return out


def xor_sum(x, axis, size):
    if size & (size - 1):
        return lax.psum(x, axis)
    index = lax.axis_index(axis)
    bits = [1 << k for k in range(size.bit_length() - 1)][::-1]
    for group in bit_groups(bits):
        mask = sum(group)
        stacked = xor_round(x, axis, size, group)
        order = [counter_of((v ^ (index & mask)), group) for v in range(mask + 1) if v & ~mask == 0]
        terms = [stacked[k] for k in order]
        while len(terms) > 1:
            terms = [terms[i] + terms[i + 1] for i in range(0, len(terms), 2)]
        x = terms[0]
    return x


def ordered_gather(block, owners, readers):
    reader_index = lax.axis_index("reader")
    owner_index = lax.axis_index("owner") if owners > 1 else 0
    group_size = readers // owners
    bits = [1 << k for k in range(readers.bit_length() - 1)][::-1]
    target = owner_index * group_size
    held = block[None]
    for group in bit_groups(bits):
        high = sum(bit for bit in group if bit >= group_size)
        low = [bit for bit in group if bit < group_size]
        stacked = xor_round(held, "reader", readers, group)
        c_high = (reader_index ^ target) & high
        picks = []
        values = sorted(sum(bit for k, bit in enumerate(low) if count >> k & 1) for count in range(1 << len(low)))
        for v in values:
            c = c_high + (v ^ (reader_index & sum(low)))
            picks.append(counter_of(c, group))
        chosen = jnp.take(stacked, jnp.stack(picks), axis=0)
        chosen = jnp.swapaxes(chosen, 0, 1)
        held = chosen.reshape((-1,) + block.shape)
    return held


def half_gather(block, owners, readers):
    held = ordered_gather(block, owners, readers)
    return jnp.transpose(held, (1, 0, 2)).reshape(block.shape[0], -1)


def local(acts, grads, basis_a, basis_g, eigvals, lengths, shuffle):
    owners = lax.axis_size("owner")
    readers = lax.axis_size("reader")
    owner_index = lax.axis_index("owner")
    rows = acts.shape[0] * readers
    slots = rows // SEQ
    m_block = basis_g.shape[0]
    n_block = basis_a.shape[0]
    width = eigvals.shape[1]
    dim_ff = m_block * readers
    dim_d = width * owners

    all_g = lax.all_gather(grads, "reader", axis=0, tiled=True)
    all_a = ordered_gather(acts, 1, readers).reshape(rows, acts.shape[1])

    token = jnp.arange(rows, dtype=jnp.int32)
    live = ((token % SEQ) < lengths[token // SEQ]).astype(jnp.float32)

    part_a = jnp.einsum("tk,jk->tj", all_a, basis_a, preferred_element_type=jnp.float32)
    rot_a_block = (xor_sum(part_a, "owner", owners) * live[:, None]).astype(jnp.bfloat16)
    pieces = []
    step = m_block // 2
    for start in range(0, m_block, step):
        part_g = jnp.einsum(
            "tk,jk->tj", all_g, basis_g[start:start + step], preferred_element_type=jnp.float32
        )
        pieces.append(xor_sum(part_g, "owner", owners))
    rot_g = (jnp.concatenate(pieces, axis=1) * live[:, None]).astype(jnp.bfloat16)

    rot_a = half_gather(rot_a_block, owners, readers)

    denom = eigvals.astype(jnp.float32)
    g_rows = rot_g.reshape(slots, SEQ, m_block)
    a_rows = rot_a.reshape(slots, SEQ, width)
    outer = jnp.einsum("smt,smn->stn", g_rows, a_rows, preferred_element_type=jnp.float32)
    scaled = (outer / denom[None]).astype(jnp.bfloat16)
    projected = jnp.einsum("stm,smn->stn", g_rows, scaled, preferred_element_type=jnp.float32)
    partial = jnp.sum(projected * a_rows.astype(jnp.float32), axis=2) / (dim_ff * dim_d)
    scores = xor_sum(xor_sum(partial, "reader", readers), "owner", owners)

    token_score = lax.dynamic_index_in_dim(scores, owner_index, 0, keepdims=False)
    slot_mean = jnp.sum(scores, axis=1) / SEQ
    table = (shuffle[:, None] == jnp.arange(slots, dtype=jnp.int32)[None, :]).astype(jnp.float32)
    example_score = jnp.sum(slot_mean[:, None] * table, axis=0)
    return (token_score, example_score)


def solution(mesh):
    return jax.shard_map(
        local,
        mesh=mesh,
        in_specs=(
            P("reader", "owner"),
            P("reader", "owner"),
            P("reader", "owner"),
            P("reader", "owner"),
            P("reader", "owner"),
            P(),
            P(),
        ),
        out_specs=(P("owner"), P()),
        check_vma=False,
    )
```

```python
import jax
import jax.numpy as jnp
from jax import lax
from jax.sharding import PartitionSpec as P

SEQ = 128


def bit_groups(bits):
    return [bits[i:i + 2] for i in range(0, len(bits), 2)]


def xor_round(held, axis, size, group):
    parts = [held]
    for count in range(1, 1 << len(group)):
        c = sum(bit for k, bit in enumerate(group) if count >> k & 1)
        parts.append(lax.ppermute(held, axis, [(i, i ^ c) for i in range(size)]))
    return jnp.stack(parts)


def counter_of(c, group):
    out = jnp.zeros_like(c)
    for k, bit in enumerate(group):
        out = out + (((c >> (bit.bit_length() - 1)) & 1) << k)
    return out


def xor_sum(x, axis, size):
    if size & (size - 1):
        return lax.psum(x, axis)
    index = lax.axis_index(axis)
    bits = [1 << k for k in range(size.bit_length() - 1)][::-1]
    for group in bit_groups(bits):
        mask = sum(group)
        stacked = xor_round(x, axis, size, group)
        order = [counter_of((v ^ (index & mask)), group) for v in range(mask + 1) if v & ~mask == 0]
        terms = [stacked[k] for k in order]
        while len(terms) > 1:
            terms = [terms[i] + terms[i + 1] for i in range(0, len(terms), 2)]
        x = terms[0]
    return x


def ordered_gather(block, owners, readers):
    reader_index = lax.axis_index("reader")
    owner_index = lax.axis_index("owner") if owners > 1 else 0
    group_size = readers // owners
    bits = [1 << k for k in range(readers.bit_length() - 1)][::-1]
    target = owner_index * group_size
    held = block[None]
    for group in bit_groups(bits):
        high = sum(bit for bit in group if bit >= group_size)
        low = [bit for bit in group if bit < group_size]
        stacked = xor_round(held, "reader", readers, group)
        c_high = (reader_index ^ target) & high
        picks = []
        values = sorted(sum(bit for k, bit in enumerate(low) if count >> k & 1) for count in range(1 << len(low)))
        for v in values:
            c = c_high + (v ^ (reader_index & sum(low)))
            picks.append(counter_of(c, group))
        chosen = jnp.take(stacked, jnp.stack(picks), axis=0)
        chosen = jnp.swapaxes(chosen, 0, 1)
        held = chosen.reshape((-1,) + block.shape)
    return held


def row_rounds(rows_block, readers):
    bits = [1 << k for k in range(readers.bit_length() - 1)][::-1]
    groups = bit_groups([bit for bit in bits if bit >= 4]) + [[bit] for bit in bits if bit < 4]
    held = rows_block[None]
    offsets = [0]
    pieces = [(held, [0])]
    for group in groups:
        received = []
        new_offsets = []
        for count in range(1, 1 << len(group)):
            c = sum(bit for k, bit in enumerate(group) if count >> k & 1)
            received.append(lax.ppermute(held, "reader", [(i, i ^ c) for i in range(readers)]))
            new_offsets += [c ^ o for o in offsets]
        piece = jnp.concatenate(received, axis=0)
        pieces.append((piece, new_offsets))
        held = jnp.concatenate([held, piece], axis=0)
        offsets = offsets + new_offsets
    return pieces, offsets


def half_gather(block, owners, readers):
    held = ordered_gather(block, owners, readers)
    return jnp.transpose(held, (1, 0, 2)).reshape(block.shape[0], -1)


def local(acts, grads, basis_a, basis_g, eigvals, lengths, shuffle):
    owners = lax.axis_size("owner")
    readers = lax.axis_size("reader")
    owner_index = lax.axis_index("owner")
    rows = acts.shape[0] * readers
    slots = rows // SEQ
    m_block = basis_g.shape[0]
    n_block = basis_a.shape[0]
    width = eigvals.shape[1]
    dim_ff = m_block * readers
    dim_d = width * owners

    joined = jnp.concatenate([grads, acts], axis=1)
    pieces, offsets = row_rounds(joined, readers)
    width_g = grads.shape[1]
    summed = []
    for piece, _ in pieces:
        flat = piece.reshape(-1, piece.shape[-1])
        part_a = jnp.einsum("tk,jk->tj", flat[:, width_g:], basis_a, preferred_element_type=jnp.float32)
        part_g = jnp.einsum("tk,jk->tj", flat[:, :width_g], basis_g, preferred_element_type=jnp.float32)
        part = jnp.concatenate([part_g, part_a], axis=1)
        summed.append(xor_sum(part, "owner", owners))
    whole = jnp.concatenate(summed, axis=0).reshape(readers, acts.shape[0], -1)
    position = [0] * readers
    for p, off in enumerate(offsets):
        position[off] = p
    reader_index = lax.axis_index("reader")
    order = jnp.asarray(position, jnp.int32)[reader_index ^ jnp.arange(readers, dtype=jnp.int32)]
    whole = jnp.take(whole, order, axis=0).reshape(rows, -1)

    token = jnp.arange(rows, dtype=jnp.int32)
    live = ((token % SEQ) < lengths[token // SEQ]).astype(jnp.float32)
    rot = (whole * live[:, None]).astype(jnp.bfloat16)
    rot_g = rot[:, :m_block]
    rot_a_block = rot[:, m_block:]

    rot_a = half_gather(rot_a_block, owners, readers)

    denom = eigvals.astype(jnp.float32)
    g_rows = rot_g.reshape(slots, SEQ, m_block)
    a_rows = rot_a.reshape(slots, SEQ, width)
    outer = jnp.einsum("smt,smn->stn", g_rows, a_rows, preferred_element_type=jnp.float32)
    scaled = (outer / denom[None]).astype(jnp.bfloat16)
    projected = jnp.einsum("stm,smn->stn", g_rows, scaled, preferred_element_type=jnp.float32)
    partial = jnp.sum(projected * a_rows.astype(jnp.float32), axis=2) / (dim_ff * dim_d)
    scores = xor_sum(xor_sum(partial, "reader", readers), "owner", owners)

    token_score = lax.dynamic_index_in_dim(scores, owner_index, 0, keepdims=False)
    slot_mean = jnp.sum(scores, axis=1) / SEQ
    table = (shuffle[:, None] == jnp.arange(slots, dtype=jnp.int32)[None, :]).astype(jnp.float32)
    example_score = jnp.sum(slot_mean[:, None] * table, axis=0)
    return (token_score, example_score)


def solution(mesh):
    return jax.shard_map(
        local,
        mesh=mesh,
        in_specs=(
            P("reader", "owner"),
            P("reader", "owner"),
            P("reader", "owner"),
            P("reader", "owner"),
            P("reader", "owner"),
            P(),
            P(),
        ),
        out_specs=(P("owner"), P()),
        check_vma=False,
    )
```

```python
import jax
import jax.numpy as jnp
from jax import lax
from jax.sharding import PartitionSpec as P

SEQ = 128


def bit_groups(bits):
    return [bits[i:i + 2] for i in range(0, len(bits), 2)]


def xor_round(held, axis, size, group):
    parts = [held]
    for count in range(1, 1 << len(group)):
        c = sum(bit for k, bit in enumerate(group) if count >> k & 1)
        parts.append(lax.ppermute(held, axis, [(i, i ^ c) for i in range(size)]))
    return jnp.stack(parts)


def counter_of(c, group):
    out = jnp.zeros_like(c)
    for k, bit in enumerate(group):
        out = out + (((c >> (bit.bit_length() - 1)) & 1) << k)
    return out


def xor_sum(x, axis, size):
    if size & (size - 1):
        return lax.psum(x, axis)
    index = lax.axis_index(axis)
    bits = [1 << k for k in range(size.bit_length() - 1)][::-1]
    for group in bit_groups(bits):
        mask = sum(group)
        stacked = xor_round(x, axis, size, group)
        order = [counter_of((v ^ (index & mask)), group) for v in range(mask + 1) if v & ~mask == 0]
        terms = [stacked[k] for k in order]
        while len(terms) > 1:
            terms = [terms[i] + terms[i + 1] for i in range(0, len(terms), 2)]
        x = terms[0]
    return x


def ordered_gather(block, owners, readers):
    reader_index = lax.axis_index("reader")
    owner_index = lax.axis_index("owner") if owners > 1 else 0
    group_size = readers // owners
    bits = [1 << k for k in range(readers.bit_length() - 1)][::-1]
    target = owner_index * group_size
    held = block[None]
    for group in bit_groups(bits):
        high = sum(bit for bit in group if bit >= group_size)
        low = [bit for bit in group if bit < group_size]
        stacked = xor_round(held, "reader", readers, group)
        c_high = (reader_index ^ target) & high
        picks = []
        values = sorted(sum(bit for k, bit in enumerate(low) if count >> k & 1) for count in range(1 << len(low)))
        for v in values:
            c = c_high + (v ^ (reader_index & sum(low)))
            picks.append(counter_of(c, group))
        chosen = jnp.take(stacked, jnp.stack(picks), axis=0)
        chosen = jnp.swapaxes(chosen, 0, 1)
        held = chosen.reshape((-1,) + block.shape)
    return held


def half_gather(block, owners, readers):
    held = ordered_gather(block, owners, readers)
    return jnp.transpose(held, (1, 0, 2)).reshape(block.shape[0], -1)


def local(acts, grads, basis_a, basis_g, eigvals, lengths, shuffle):
    owners = lax.axis_size("owner")
    readers = lax.axis_size("reader")
    owner_index = lax.axis_index("owner")
    rows = acts.shape[0] * readers
    slots = rows // SEQ
    m_block = basis_g.shape[0]
    n_block = basis_a.shape[0]
    width = eigvals.shape[1]
    dim_ff = m_block * readers
    dim_d = width * owners

    all_g = lax.all_gather(grads, "reader", axis=0, tiled=True)
    all_a = ordered_gather(acts, 1, readers).reshape(rows, acts.shape[1])

    token = jnp.arange(rows, dtype=jnp.int32)
    live = ((token % SEQ) < lengths[token // SEQ]).astype(jnp.float32)

    part_a = jnp.einsum("tk,jk->tj", all_a, basis_a, preferred_element_type=jnp.float32)
    rot_a_block = (xor_sum(part_a, "owner", owners) * live[:, None]).astype(jnp.bfloat16)
    pieces = []
    step = m_block // 4
    for start in range(0, m_block, step):
        part_g = jnp.einsum(
            "tk,jk->tj", all_g, basis_g[start:start + step], preferred_element_type=jnp.float32
        )
        pieces.append((xor_sum(part_g, "owner", owners) * live[:, None]).astype(jnp.bfloat16))
    rot_g = jnp.concatenate(pieces, axis=1)

    rot_a = half_gather(rot_a_block, owners, readers)

    denom = eigvals.astype(jnp.float32)
    g_rows = rot_g.reshape(slots, SEQ, m_block)
    a_rows = rot_a.reshape(slots, SEQ, width)
    outer = jnp.einsum("smt,smn->stn", g_rows, a_rows, preferred_element_type=jnp.float32)
    scaled = (outer / denom[None]).astype(jnp.bfloat16)
    projected = jnp.einsum("stm,smn->stn", g_rows, scaled, preferred_element_type=jnp.float32)
    partial = jnp.sum(projected * a_rows.astype(jnp.float32), axis=2) / (dim_ff * dim_d)
    scores = xor_sum(xor_sum(partial, "reader", readers), "owner", owners)

    token_score = lax.dynamic_index_in_dim(scores, owner_index, 0, keepdims=False)
    slot_mean = jnp.sum(scores, axis=1) / SEQ
    table = (shuffle[:, None] == jnp.arange(slots, dtype=jnp.int32)[None, :]).astype(jnp.float32)
    example_score = jnp.sum(slot_mean[:, None] * table, axis=0)
    return (token_score, example_score)


def solution(mesh):
    return jax.shard_map(
        local,
        mesh=mesh,
        in_specs=(
            P("reader", "owner"),
            P("reader", "owner"),
            P("reader", "owner"),
            P("reader", "owner"),
            P("reader", "owner"),
            P(),
            P(),
        ),
        out_specs=(P("owner"), P()),
        check_vma=False,
    )
```

```python
import jax
import jax.numpy as jnp
from jax import lax
from jax.sharding import PartitionSpec as P

SEQ = 128


def bit_groups(bits):
    return [bits[i:i + 2] for i in range(0, len(bits), 2)]


def xor_round(held, axis, size, group):
    parts = [held]
    for count in range(1, 1 << len(group)):
        c = sum(bit for k, bit in enumerate(group) if count >> k & 1)
        parts.append(lax.ppermute(held, axis, [(i, i ^ c) for i in range(size)]))
    return jnp.stack(parts)


def counter_of(c, group):
    out = jnp.zeros_like(c)
    for k, bit in enumerate(group):
        out = out + (((c >> (bit.bit_length() - 1)) & 1) << k)
    return out


def xor_sum(x, axis, size):
    if size & (size - 1):
        return lax.psum(x, axis)
    index = lax.axis_index(axis)
    bits = [1 << k for k in range(size.bit_length() - 1)][::-1]
    for group in bit_groups(bits):
        mask = sum(group)
        stacked = xor_round(x, axis, size, group)
        order = [counter_of((v ^ (index & mask)), group) for v in range(mask + 1) if v & ~mask == 0]
        terms = [stacked[k] for k in order]
        while len(terms) > 1:
            terms = [terms[i] + terms[i + 1] for i in range(0, len(terms), 2)]
        x = terms[0]
    return x


def ordered_gather(block, owners, readers, after=None):
    reader_index = lax.axis_index("reader")
    owner_index = lax.axis_index("owner") if owners > 1 else 0
    group_size = readers // owners
    bits = [1 << k for k in range(readers.bit_length() - 1)][::-1]
    target = owner_index * group_size
    held = block[None]
    groups = bit_groups(bits)
    for group in groups:
        high = sum(bit for bit in group if bit >= group_size)
        low = [bit for bit in group if bit < group_size]
        if after is not None and group is groups[-1]:
            held, _ = lax.optimization_barrier((held, after))
        stacked = xor_round(held, "reader", readers, group)
        c_high = (reader_index ^ target) & high
        picks = []
        values = sorted(sum(bit for k, bit in enumerate(low) if count >> k & 1) for count in range(1 << len(low)))
        for v in values:
            c = c_high + (v ^ (reader_index & sum(low)))
            picks.append(counter_of(c, group))
        chosen = jnp.take(stacked, jnp.stack(picks), axis=0)
        chosen = jnp.swapaxes(chosen, 0, 1)
        held = chosen.reshape((-1,) + block.shape)
    return held


def half_gather(block, owners, readers, after):
    held = ordered_gather(block, owners, readers, after)
    return jnp.transpose(held, (1, 0, 2)).reshape(block.shape[0], -1)


def local(acts, grads, basis_a, basis_g, eigvals, lengths, shuffle):
    owners = lax.axis_size("owner")
    readers = lax.axis_size("reader")
    owner_index = lax.axis_index("owner")
    rows = acts.shape[0] * readers
    slots = rows // SEQ
    m_block = basis_g.shape[0]
    n_block = basis_a.shape[0]
    width = eigvals.shape[1]
    dim_ff = m_block * readers
    dim_d = width * owners

    all_g = lax.all_gather(grads, "reader", axis=0, tiled=True)
    all_a = ordered_gather(acts, 1, readers).reshape(rows, acts.shape[1])

    token = jnp.arange(rows, dtype=jnp.int32)
    live = ((token % SEQ) < lengths[token // SEQ]).astype(jnp.float32)

    part_a = jnp.einsum("tk,jk->tj", all_a, basis_a, preferred_element_type=jnp.float32)
    rot_a_block = (xor_sum(part_a, "owner", owners) * live[:, None]).astype(jnp.bfloat16)
    step = m_block // 4
    parts_g = [
        jnp.einsum("tk,jk->tj", all_g, basis_g[start:start + step], preferred_element_type=jnp.float32)
        for start in range(0, m_block, step)
    ]
    parts_g[0], eig_after = lax.optimization_barrier((parts_g[0], eigvals))
    pieces = [(xor_sum(part_g, "owner", owners) * live[:, None]).astype(jnp.bfloat16) for part_g in parts_g]
    rot_g = jnp.concatenate(pieces, axis=1)

    rot_a = half_gather(rot_a_block, owners, readers, parts_g[0])

    denom = eig_after.astype(jnp.float32)
    g_rows = rot_g.reshape(slots, SEQ, m_block)
    a_rows = rot_a.reshape(slots, SEQ, width)
    outer = jnp.einsum("smt,smn->stn", g_rows, a_rows, preferred_element_type=jnp.float32)
    scaled = (outer / denom[None]).astype(jnp.bfloat16)
    projected = jnp.einsum("stm,smn->stn", g_rows, scaled, preferred_element_type=jnp.float32)
    partial = jnp.sum(projected * a_rows.astype(jnp.float32), axis=2) / (dim_ff * dim_d)
    scores = xor_sum(xor_sum(partial, "reader", readers), "owner", owners)

    token_score = lax.dynamic_index_in_dim(scores, owner_index, 0, keepdims=False)
    slot_mean = jnp.sum(scores, axis=1) / SEQ
    table = (shuffle[:, None] == jnp.arange(slots, dtype=jnp.int32)[None, :]).astype(jnp.float32)
    example_score = jnp.sum(slot_mean[:, None] * table, axis=0)
    return (token_score, example_score)


def solution(mesh):
    return jax.shard_map(
        local,
        mesh=mesh,
        in_specs=(
            P("reader", "owner"),
            P("reader", "owner"),
            P("reader", "owner"),
            P("reader", "owner"),
            P("reader", "owner"),
            P(),
            P(),
        ),
        out_specs=(P("owner"), P()),
        check_vma=False,
    )
```

```python
import jax
import jax.numpy as jnp
from jax import lax
from jax.sharding import PartitionSpec as P

SEQ = 128
READER = ("rz", "rc")


def bit_groups(bits):
    return [bits[i:i + 2] for i in range(0, len(bits), 2)]


def xor_round(held, axis, size, group):
    parts = [held]
    for count in range(1, 1 << len(group)):
        c = sum(bit for k, bit in enumerate(group) if count >> k & 1)
        parts.append(lax.ppermute(held, axis, [(i, i ^ c) for i in range(size)]))
    return jnp.stack(parts)


def counter_of(c, group):
    out = jnp.zeros_like(c)
    for k, bit in enumerate(group):
        out = out + (((c >> (bit.bit_length() - 1)) & 1) << k)
    return out


def xor_sum(x, axis, size):
    if size & (size - 1):
        return lax.psum(x, axis)
    index = lax.axis_index(axis)
    bits = [1 << k for k in range(size.bit_length() - 1)][::-1]
    for group in bit_groups(bits):
        mask = sum(group)
        stacked = xor_round(x, axis, size, group)
        order = [counter_of((v ^ (index & mask)), group) for v in range(mask + 1) if v & ~mask == 0]
        terms = [stacked[k] for k in order]
        while len(terms) > 1:
            terms = [terms[i] + terms[i + 1] for i in range(0, len(terms), 2)]
        x = terms[0]
    return x


def ordered_gather(block, owners, readers):
    reader_index = lax.axis_index(READER)
    owner_index = lax.axis_index("owner") if owners > 1 else 0
    group_size = readers // owners
    bits = [1 << k for k in range(readers.bit_length() - 1)][::-1]
    target = owner_index * group_size
    held = block[None]
    for group in bit_groups(bits):
        high = sum(bit for bit in group if bit >= group_size)
        low = [bit for bit in group if bit < group_size]
        stacked = xor_round(held, READER, readers, group)
        c_high = (reader_index ^ target) & high
        picks = []
        values = sorted(sum(bit for k, bit in enumerate(low) if count >> k & 1) for count in range(1 << len(low)))
        for v in values:
            c = c_high + (v ^ (reader_index & sum(low)))
            picks.append(counter_of(c, group))
        chosen = jnp.take(stacked, jnp.stack(picks), axis=0)
        chosen = jnp.swapaxes(chosen, 0, 1)
        held = chosen.reshape((-1,) + block.shape)
    return held


def half_gather(block, owners, readers):
    held = ordered_gather(block, owners, readers)
    return jnp.transpose(held, (1, 0, 2)).reshape(block.shape[0], -1)


def local(acts, grads, basis_a, basis_g, eigvals, lengths, shuffle):
    owners = lax.axis_size("owner")
    halves = lax.axis_size("rc")
    readers = lax.axis_size("rz") * halves
    owner_index = lax.axis_index("owner")
    rows = acts.shape[0] * readers
    slots = rows // SEQ
    m_block = basis_g.shape[0]
    n_block = basis_a.shape[0]
    width = eigvals.shape[1]
    dim_ff = m_block * readers
    dim_d = width * owners

    joined = jnp.concatenate([grads, acts], axis=1)
    near = lax.all_gather(joined, "rz", axis=0, tiled=True)
    parts = [near] + [
        lax.ppermute(near, "rc", [(i, (i + shift) % halves) for i in range(halves)])
        for shift in range(1, halves)
    ]
    rel = jnp.concatenate(parts, axis=0)
    all_g = rel[:, : grads.shape[1]]
    all_a = rel[:, grads.shape[1]:]

    half_index = lax.axis_index("rc")
    block = jnp.arange(readers, dtype=jnp.int32)
    rz_of = block % (readers // halves)
    rc_of = (half_index - block // (readers // halves)) % halves
    source = rz_of * halves + rc_of
    token = (source[:, None] * acts.shape[0] + jnp.arange(acts.shape[0], dtype=jnp.int32)[None, :]).reshape(rows)
    live = ((token % SEQ) < lengths[token // SEQ]).astype(jnp.float32)
    position = ((half_index - block % halves) % halves) * (readers // halves) + block // halves

    def in_token_order(x):
        return jnp.take(x.reshape(readers, acts.shape[0], -1), position, axis=0).reshape(rows, -1)

    part_a = jnp.einsum("tk,jk->tj", all_a, basis_a, preferred_element_type=jnp.float32)
    rot_a_block = in_token_order((xor_sum(part_a, "owner", owners) * live[:, None]).astype(jnp.bfloat16))
    pieces = []
    step = m_block // 2
    for start in range(0, m_block, step):
        part_g = jnp.einsum(
            "tk,jk->tj", all_g, basis_g[start:start + step], preferred_element_type=jnp.float32
        )
        pieces.append(xor_sum(part_g, "owner", owners))
    rot_g = in_token_order((jnp.concatenate(pieces, axis=1) * live[:, None]).astype(jnp.bfloat16))

    rot_a = half_gather(rot_a_block, owners, readers)

    denom = eigvals.astype(jnp.float32)
    g_rows = rot_g.reshape(slots, SEQ, m_block)
    a_rows = rot_a.reshape(slots, SEQ, width)
    outer = jnp.einsum("smt,smn->stn", g_rows, a_rows, preferred_element_type=jnp.float32)
    scaled = (outer / denom[None]).astype(jnp.bfloat16)
    projected = jnp.einsum("stm,smn->stn", g_rows, scaled, preferred_element_type=jnp.float32)
    partial = jnp.sum(projected * a_rows.astype(jnp.float32), axis=2) / (dim_ff * dim_d)
    scores = xor_sum(xor_sum(partial, READER, readers), "owner", owners)

    token_score = lax.dynamic_index_in_dim(scores, owner_index, 0, keepdims=False)
    slot_mean = jnp.sum(scores, axis=1) / SEQ
    table = (shuffle[:, None] == jnp.arange(slots, dtype=jnp.int32)[None, :]).astype(jnp.float32)
    example_score = jnp.sum(slot_mean[:, None] * table, axis=0)
    return (token_score, example_score)


def solution(mesh):
    owners, readers = mesh.devices.shape
    split = jax.sharding.Mesh(mesh.devices.reshape(owners, readers // 2, 2), ("owner",) + READER)
    rows = P(READER, "owner")
    return jax.shard_map(
        local,
        mesh=split,
        in_specs=(rows, rows, rows, rows, rows, P(), P()),
        out_specs=(P("owner"), P()),
        check_vma=False,
    )
```

```python
import jax
import jax.numpy as jnp
from jax import lax
from jax.sharding import PartitionSpec as P

SEQ = 128


def bit_groups(bits):
    return [bits[i:i + 2] for i in range(0, len(bits), 2)]


def xor_round(held, axis, size, group):
    parts = [held]
    for count in range(1, 1 << len(group)):
        c = sum(bit for k, bit in enumerate(group) if count >> k & 1)
        parts.append(lax.ppermute(held, axis, [(i, i ^ c) for i in range(size)]))
    return jnp.stack(parts)


def counter_of(c, group):
    out = jnp.zeros_like(c)
    for k, bit in enumerate(group):
        out = out + (((c >> (bit.bit_length() - 1)) & 1) << k)
    return out


def xor_sum(x, axis, size):
    if size & (size - 1):
        return lax.psum(x, axis)
    index = lax.axis_index(axis)
    bits = [1 << k for k in range(size.bit_length() - 1)][::-1]
    for group in bit_groups(bits):
        mask = sum(group)
        stacked = xor_round(x, axis, size, group)
        order = [counter_of((v ^ (index & mask)), group) for v in range(mask + 1) if v & ~mask == 0]
        terms = [stacked[k] for k in order]
        while len(terms) > 1:
            terms = [terms[i] + terms[i + 1] for i in range(0, len(terms), 2)]
        x = terms[0]
    return x


def ordered_gather(block, owners, readers):
    reader_index = lax.axis_index("reader")
    owner_index = lax.axis_index("owner") if owners > 1 else 0
    group_size = readers // owners
    bits = [1 << k for k in range(readers.bit_length() - 1)][::-1]
    target = owner_index * group_size
    held = block[None]
    for group in bit_groups(bits):
        high = sum(bit for bit in group if bit >= group_size)
        low = [bit for bit in group if bit < group_size]
        stacked = xor_round(held, "reader", readers, group)
        c_high = (reader_index ^ target) & high
        picks = []
        values = sorted(sum(bit for k, bit in enumerate(low) if count >> k & 1) for count in range(1 << len(low)))
        for v in values:
            c = c_high + (v ^ (reader_index & sum(low)))
            picks.append(counter_of(c, group))
        chosen = jnp.take(stacked, jnp.stack(picks), axis=0)
        chosen = jnp.swapaxes(chosen, 0, 1)
        held = chosen.reshape((-1,) + block.shape)
    return held


def half_gather(block, owners, readers):
    held = ordered_gather(block, owners, readers)
    return jnp.transpose(held, (1, 0, 2)).reshape(block.shape[0], -1)


def local(acts, grads, basis_a, basis_g, eigvals, lengths, shuffle):
    owners = lax.axis_size("owner")
    readers = lax.axis_size("reader")
    owner_index = lax.axis_index("owner")
    rows = acts.shape[0] * readers
    slots = rows // SEQ
    m_block = basis_g.shape[0]
    n_block = basis_a.shape[0]
    width = eigvals.shape[1]
    dim_ff = m_block * readers
    dim_d = width * owners

    all_g = lax.all_gather(grads, "reader", axis=0, tiled=True)
    all_a = ordered_gather(acts, 1, readers).reshape(rows, acts.shape[1])

    token = jnp.arange(rows, dtype=jnp.int32)
    live = ((token % SEQ) < lengths[token // SEQ]).astype(jnp.float32)

    part_a = jnp.einsum("tk,jk->tj", all_a, basis_a, preferred_element_type=jnp.float32)
    rot_a_block = (xor_sum(part_a, "owner", owners) * live[:, None]).astype(jnp.bfloat16)
    pieces = []
    step = m_block // 2
    for start in range(0, m_block, step):
        part_g = jnp.einsum(
            "tk,jk->tj", all_g, basis_g[start:start + step], preferred_element_type=jnp.float32
        )
        pieces.append((xor_sum(part_g, "owner", owners) * live[:, None]).astype(jnp.bfloat16))
    rot_g = jnp.concatenate(pieces, axis=1)

    rot_a = half_gather(rot_a_block, owners, readers)

    denom = eigvals.astype(jnp.float32)
    g_rows = rot_g.reshape(slots, SEQ, m_block)
    a_rows = rot_a.reshape(slots, SEQ, width)
    outer = jnp.einsum("smt,smn->stn", g_rows, a_rows, preferred_element_type=jnp.float32)
    scaled = (outer / denom[None]).astype(jnp.bfloat16)
    projected = jnp.einsum("stm,smn->stn", g_rows, scaled, preferred_element_type=jnp.float32)
    partial = jnp.sum(projected * a_rows.astype(jnp.float32), axis=2) / (dim_ff * dim_d)
    scores = xor_sum(xor_sum(partial, "reader", readers), "owner", owners)

    token_score = lax.dynamic_index_in_dim(scores, owner_index, 0, keepdims=False)
    slot_mean = jnp.sum(scores, axis=1) / SEQ
    table = (shuffle[:, None] == jnp.arange(slots, dtype=jnp.int32)[None, :]).astype(jnp.float32)
    example_score = jnp.sum(slot_mean[:, None] * table, axis=0)
    return (token_score, example_score)


def solution(mesh):
    return jax.shard_map(
        local,
        mesh=mesh,
        in_specs=(
            P("reader", "owner"),
            P("reader", "owner"),
            P("reader", "owner"),
            P("reader", "owner"),
            P("reader", "owner"),
            P(),
            P(),
        ),
        out_specs=(P("owner"), P()),
        check_vma=False,
    )
```

```python
import jax
import jax.numpy as jnp
from jax import lax
from jax.sharding import PartitionSpec as P

SEQ = 128


def bit_groups(bits):
    return [bits[i:i + 2] for i in range(0, len(bits), 2)]


def xor_round(held, axis, size, group):
    parts = [held]
    for count in range(1, 1 << len(group)):
        c = sum(bit for k, bit in enumerate(group) if count >> k & 1)
        parts.append(lax.ppermute(held, axis, [(i, i ^ c) for i in range(size)]))
    return jnp.stack(parts)


def counter_of(c, group):
    out = jnp.zeros_like(c)
    for k, bit in enumerate(group):
        out = out + (((c >> (bit.bit_length() - 1)) & 1) << k)
    return out


def xor_sum(x, axis, size):
    if size & (size - 1):
        return lax.psum(x, axis)
    index = lax.axis_index(axis)
    bits = [1 << k for k in range(size.bit_length() - 1)][::-1]
    for group in bit_groups(bits):
        mask = sum(group)
        stacked = xor_round(x, axis, size, group)
        order = [counter_of((v ^ (index & mask)), group) for v in range(mask + 1) if v & ~mask == 0]
        terms = [stacked[k] for k in order]
        while len(terms) > 1:
            terms = [terms[i] + terms[i + 1] for i in range(0, len(terms), 2)]
        x = terms[0]
    return x


def ordered_gather(block, owners, readers):
    reader_index = lax.axis_index("reader")
    owner_index = lax.axis_index("owner") if owners > 1 else 0
    group_size = readers // owners
    bits = [1 << k for k in range(readers.bit_length() - 1)][::-1]
    target = owner_index * group_size
    held = block[None]
    for group in bit_groups(bits):
        high = sum(bit for bit in group if bit >= group_size)
        low = [bit for bit in group if bit < group_size]
        stacked = xor_round(held, "reader", readers, group)
        c_high = (reader_index ^ target) & high
        picks = []
        values = sorted(sum(bit for k, bit in enumerate(low) if count >> k & 1) for count in range(1 << len(low)))
        for v in values:
            c = c_high + (v ^ (reader_index & sum(low)))
            picks.append(counter_of(c, group))
        chosen = jnp.take(stacked, jnp.stack(picks), axis=0)
        chosen = jnp.swapaxes(chosen, 0, 1)
        held = chosen.reshape((-1,) + block.shape)
    return held


def half_gather(block, owners, readers):
    held = ordered_gather(block, owners, readers)
    return jnp.transpose(held, (1, 0, 2)).reshape(block.shape[0], -1)


def local(acts, grads, basis_a, basis_g, eigvals, lengths, shuffle):
    owners = lax.axis_size("owner")
    readers = lax.axis_size("reader")
    owner_index = lax.axis_index("owner")
    rows = acts.shape[0] * readers
    slots = rows // SEQ
    m_block = basis_g.shape[0]
    n_block = basis_a.shape[0]
    width = eigvals.shape[1]
    dim_ff = m_block * readers
    dim_d = width * owners

    all_g = lax.all_gather(grads, "reader", axis=0, tiled=True)
    all_a = ordered_gather(acts, 1, readers).reshape(rows, acts.shape[1])

    token = jnp.arange(rows, dtype=jnp.int32)
    live = ((token % SEQ) < lengths[token // SEQ]).astype(jnp.float32)

    part_a = jnp.einsum("tk,jk->tj", all_a, basis_a, preferred_element_type=jnp.float32)
    rot_a_block = (xor_sum(part_a, "owner", owners) * live[:, None]).astype(jnp.bfloat16)
    pieces = []
    step = m_block // 2
    for start in range(0, m_block, step):
        part_g = jnp.einsum(
            "tk,jk->tj", all_g, basis_g[start:start + step], preferred_element_type=jnp.float32
        )
        pieces.append((xor_sum(part_g, "owner", owners) * live[:, None]).astype(jnp.bfloat16))
    rot_g = jnp.concatenate(pieces, axis=1)

    rot_a = half_gather(rot_a_block, owners, readers)

    g_rows = rot_g.reshape(slots, SEQ, m_block)
    a_rows = rot_a.reshape(slots, SEQ, width)
    partials = []
    for slot in range(slots):
        outer = jnp.dot(g_rows[slot].T, a_rows[slot], preferred_element_type=jnp.float32)
        scaled = (outer / eigvals.astype(jnp.float32)).astype(jnp.bfloat16)
        projected = jnp.dot(g_rows[slot], scaled, preferred_element_type=jnp.float32)
        partials.append(jnp.sum(projected * a_rows[slot].astype(jnp.float32), axis=1))
    partial = jnp.stack(partials) / (dim_ff * dim_d)
    scores = xor_sum(xor_sum(partial, "reader", readers), "owner", owners)

    token_score = lax.dynamic_index_in_dim(scores, owner_index, 0, keepdims=False)
    slot_mean = jnp.sum(scores, axis=1) / SEQ
    table = (shuffle[:, None] == jnp.arange(slots, dtype=jnp.int32)[None, :]).astype(jnp.float32)
    example_score = jnp.sum(slot_mean[:, None] * table, axis=0)
    return (token_score, example_score)


def solution(mesh):
    return jax.shard_map(
        local,
        mesh=mesh,
        in_specs=(
            P("reader", "owner"),
            P("reader", "owner"),
            P("reader", "owner"),
            P("reader", "owner"),
            P("reader", "owner"),
            P(),
            P(),
        ),
        out_specs=(P("owner"), P()),
        check_vma=False,
    )
```

```python
import jax
import jax.numpy as jnp
from jax import lax
from jax.sharding import PartitionSpec as P

SEQ = 128


def bit_groups(bits):
    return [bits[i:i + 2] for i in range(0, len(bits), 2)]


def xor_round(held, axis, size, group):
    parts = [held]
    for count in range(1, 1 << len(group)):
        c = sum(bit for k, bit in enumerate(group) if count >> k & 1)
        parts.append(lax.ppermute(held, axis, [(i, i ^ c) for i in range(size)]))
    return jnp.stack(parts)


def counter_of(c, group):
    out = jnp.zeros_like(c)
    for k, bit in enumerate(group):
        out = out + (((c >> (bit.bit_length() - 1)) & 1) << k)
    return out


def xor_sum(x, axis, size):
    if size & (size - 1):
        return lax.psum(x, axis)
    index = lax.axis_index(axis)
    bits = [1 << k for k in range(size.bit_length() - 1)][::-1]
    for group in bit_groups(bits):
        mask = sum(group)
        stacked = xor_round(x, axis, size, group)
        order = [counter_of((v ^ (index & mask)), group) for v in range(mask + 1) if v & ~mask == 0]
        terms = [stacked[k] for k in order]
        while len(terms) > 1:
            terms = [terms[i] + terms[i + 1] for i in range(0, len(terms), 2)]
        x = terms[0]
    return x


def ordered_gather(block, owners, readers, after=None):
    reader_index = lax.axis_index("reader")
    owner_index = lax.axis_index("owner") if owners > 1 else 0
    group_size = readers // owners
    bits = [1 << k for k in range(readers.bit_length() - 1)][::-1]
    target = owner_index * group_size
    held = block[None]
    groups = bit_groups(bits)
    for group in groups:
        high = sum(bit for bit in group if bit >= group_size)
        low = [bit for bit in group if bit < group_size]
        if after is not None and group is groups[-1]:
            held, _ = lax.optimization_barrier((held, after))
        stacked = xor_round(held, "reader", readers, group)
        c_high = (reader_index ^ target) & high
        picks = []
        values = sorted(sum(bit for k, bit in enumerate(low) if count >> k & 1) for count in range(1 << len(low)))
        for v in values:
            c = c_high + (v ^ (reader_index & sum(low)))
            picks.append(counter_of(c, group))
        chosen = jnp.take(stacked, jnp.stack(picks), axis=0)
        chosen = jnp.swapaxes(chosen, 0, 1)
        held = chosen.reshape((-1,) + block.shape)
    return held


def half_gather(block, owners, readers, after):
    held = ordered_gather(block, owners, readers, after)
    return jnp.transpose(held, (1, 0, 2)).reshape(block.shape[0], -1)


def local(acts, grads, basis_a, basis_g, eigvals, lengths, shuffle):
    owners = lax.axis_size("owner")
    readers = lax.axis_size("reader")
    owner_index = lax.axis_index("owner")
    rows = acts.shape[0] * readers
    slots = rows // SEQ
    m_block = basis_g.shape[0]
    n_block = basis_a.shape[0]
    width = eigvals.shape[1]
    dim_ff = m_block * readers
    dim_d = width * owners

    all_g = lax.all_gather(grads, "reader", axis=0, tiled=True)
    all_a = ordered_gather(acts, 1, readers).reshape(rows, acts.shape[1])

    token = jnp.arange(rows, dtype=jnp.int32)
    live = ((token % SEQ) < lengths[token // SEQ]).astype(jnp.float32)

    part_a = jnp.einsum("tk,jk->tj", all_a, basis_a, preferred_element_type=jnp.float32)
    rot_a_block = (xor_sum(part_a, "owner", owners) * live[:, None]).astype(jnp.bfloat16)
    first = min(256, m_block // 2)
    parts_g = [
        jnp.einsum("tk,jk->tj", all_g, basis_g[start:stop], preferred_element_type=jnp.float32)
        for start, stop in ((0, first), (first, m_block))
    ]
    parts_g[0], eig_after = lax.optimization_barrier((parts_g[0], eigvals))
    pieces = [(xor_sum(part_g, "owner", owners) * live[:, None]).astype(jnp.bfloat16) for part_g in parts_g]
    rot_g = jnp.concatenate(pieces, axis=1)

    rot_a = half_gather(rot_a_block, owners, readers, parts_g[0])

    denom = eig_after.astype(jnp.float32)
    g_rows = rot_g.reshape(slots, SEQ, m_block)
    a_rows = rot_a.reshape(slots, SEQ, width)
    outer = jnp.einsum("smt,smn->stn", g_rows, a_rows, preferred_element_type=jnp.float32)
    scaled = (outer / denom[None]).astype(jnp.bfloat16)
    projected = jnp.einsum("stm,smn->stn", g_rows, scaled, preferred_element_type=jnp.float32)
    partial = jnp.sum(projected * a_rows.astype(jnp.float32), axis=2) / (dim_ff * dim_d)
    scores = xor_sum(xor_sum(partial, "reader", readers), "owner", owners)

    token_score = lax.dynamic_index_in_dim(scores, owner_index, 0, keepdims=False)
    slot_mean = jnp.sum(scores, axis=1) / SEQ
    table = (shuffle[:, None] == jnp.arange(slots, dtype=jnp.int32)[None, :]).astype(jnp.float32)
    example_score = jnp.sum(slot_mean[:, None] * table, axis=0)
    return (token_score, example_score)


def solution(mesh):
    return jax.shard_map(
        local,
        mesh=mesh,
        in_specs=(
            P("reader", "owner"),
            P("reader", "owner"),
            P("reader", "owner"),
            P("reader", "owner"),
            P("reader", "owner"),
            P(),
            P(),
        ),
        out_specs=(P("owner"), P()),
        check_vma=False,
    )
```

```python
import jax
import jax.numpy as jnp
from jax import lax
from jax.sharding import PartitionSpec as P

SEQ = 128


def bit_groups(bits):
    return [bits[i:i + 2] for i in range(0, len(bits), 2)]


def xor_round(held, axis, size, group):
    parts = [held]
    for count in range(1, 1 << len(group)):
        c = sum(bit for k, bit in enumerate(group) if count >> k & 1)
        parts.append(lax.ppermute(held, axis, [(i, i ^ c) for i in range(size)]))
    return jnp.stack(parts)


def counter_of(c, group):
    out = jnp.zeros_like(c)
    for k, bit in enumerate(group):
        out = out + (((c >> (bit.bit_length() - 1)) & 1) << k)
    return out


def xor_sum(x, axis, size):
    if size & (size - 1):
        return lax.psum(x, axis)
    index = lax.axis_index(axis)
    bits = [1 << k for k in range(size.bit_length() - 1)][::-1]
    for group in bit_groups(bits):
        mask = sum(group)
        stacked = xor_round(x, axis, size, group)
        order = [counter_of((v ^ (index & mask)), group) for v in range(mask + 1) if v & ~mask == 0]
        terms = [stacked[k] for k in order]
        while len(terms) > 1:
            terms = [terms[i] + terms[i + 1] for i in range(0, len(terms), 2)]
        x = terms[0]
    return x


def ordered_gather(block, owners, readers):
    reader_index = lax.axis_index("reader")
    owner_index = lax.axis_index("owner") if owners > 1 else 0
    group_size = readers // owners
    bits = [1 << k for k in range(readers.bit_length() - 1)][::-1]
    target = owner_index * group_size
    held = block[None]
    for group in bit_groups(bits):
        high = sum(bit for bit in group if bit >= group_size)
        low = [bit for bit in group if bit < group_size]
        stacked = xor_round(held, "reader", readers, group)
        c_high = (reader_index ^ target) & high
        picks = []
        values = sorted(sum(bit for k, bit in enumerate(low) if count >> k & 1) for count in range(1 << len(low)))
        for v in values:
            c = c_high + (v ^ (reader_index & sum(low)))
            picks.append(counter_of(c, group))
        chosen = jnp.take(stacked, jnp.stack(picks), axis=0)
        chosen = jnp.swapaxes(chosen, 0, 1)
        held = chosen.reshape((-1,) + block.shape)
    return held


def half_gather(block, owners, readers):
    held = ordered_gather(block, owners, readers)
    return jnp.transpose(held, (1, 0, 2)).reshape(block.shape[0], -1)


def owner_rounded(part, live, owners):
    if owners != 2:
        return (xor_sum(part, "owner", owners) * live[:, None]).astype(jnp.bfloat16)
    owner_index = lax.axis_index("owner")
    half = part.shape[0] // 2
    mine = lax.dynamic_slice_in_dim(part, owner_index * half, half, axis=0)
    theirs = lax.dynamic_slice_in_dim(part, (1 - owner_index) * half, half, axis=0)
    received = lax.ppermute(theirs, "owner", [(0, 1), (1, 0)])
    first = jnp.where(owner_index == 0, mine, received)
    second = jnp.where(owner_index == 0, received, mine)
    live_mine = lax.dynamic_slice_in_dim(live, owner_index * half, half, axis=0)
    rounded = ((first + second) * live_mine[:, None]).astype(jnp.bfloat16)
    other = lax.ppermute(rounded, "owner", [(0, 1), (1, 0)])
    low = jnp.where(owner_index == 0, rounded, other)
    high = jnp.where(owner_index == 0, other, rounded)
    return jnp.concatenate([low, high], axis=0)


def local(acts, grads, basis_a, basis_g, eigvals, lengths, shuffle):
    owners = lax.axis_size("owner")
    readers = lax.axis_size("reader")
    owner_index = lax.axis_index("owner")
    rows = acts.shape[0] * readers
    slots = rows // SEQ
    m_block = basis_g.shape[0]
    n_block = basis_a.shape[0]
    width = eigvals.shape[1]
    dim_ff = m_block * readers
    dim_d = width * owners

    all_g = lax.all_gather(grads, "reader", axis=0, tiled=True)
    all_a = ordered_gather(acts, 1, readers).reshape(rows, acts.shape[1])

    token = jnp.arange(rows, dtype=jnp.int32)
    live = ((token % SEQ) < lengths[token // SEQ]).astype(jnp.float32)

    part_a = jnp.einsum("tk,jk->tj", all_a, basis_a, preferred_element_type=jnp.float32)
    rot_a_block = (xor_sum(part_a, "owner", owners) * live[:, None]).astype(jnp.bfloat16)
    pieces = []
    step = m_block // 2
    for start in range(0, m_block, step):
        part_g = jnp.einsum(
            "tk,jk->tj", all_g, basis_g[start:start + step], preferred_element_type=jnp.float32
        )
        pieces.append(owner_rounded(part_g, live, owners))
    rot_g = jnp.concatenate(pieces, axis=1)

    rot_a = half_gather(rot_a_block, owners, readers)

    denom = eigvals.astype(jnp.float32)
    g_rows = rot_g.reshape(slots, SEQ, m_block)
    a_rows = rot_a.reshape(slots, SEQ, width)
    outer = jnp.einsum("smt,smn->stn", g_rows, a_rows, preferred_element_type=jnp.float32)
    scaled = (outer / denom[None]).astype(jnp.bfloat16)
    projected = jnp.einsum("stm,smn->stn", g_rows, scaled, preferred_element_type=jnp.float32)
    partial = jnp.sum(projected * a_rows.astype(jnp.float32), axis=2) / (dim_ff * dim_d)
    scores = xor_sum(xor_sum(partial, "reader", readers), "owner", owners)

    token_score = lax.dynamic_index_in_dim(scores, owner_index, 0, keepdims=False)
    slot_mean = jnp.sum(scores, axis=1) / SEQ
    table = (shuffle[:, None] == jnp.arange(slots, dtype=jnp.int32)[None, :]).astype(jnp.float32)
    example_score = jnp.sum(slot_mean[:, None] * table, axis=0)
    return (token_score, example_score)


def solution(mesh):
    return jax.shard_map(
        local,
        mesh=mesh,
        in_specs=(
            P("reader", "owner"),
            P("reader", "owner"),
            P("reader", "owner"),
            P("reader", "owner"),
            P("reader", "owner"),
            P(),
            P(),
        ),
        out_specs=(P("owner"), P()),
        check_vma=False,
    )
```

```python
import jax
import jax.numpy as jnp
from jax import lax
from jax.sharding import PartitionSpec as P

SEQ = 128


def bit_groups(bits):
    return [bits[i:i + 2] for i in range(0, len(bits), 2)]


def xor_round(held, axis, size, group):
    parts = [held]
    for count in range(1, 1 << len(group)):
        c = sum(bit for k, bit in enumerate(group) if count >> k & 1)
        parts.append(lax.ppermute(held, axis, [(i, i ^ c) for i in range(size)]))
    return jnp.stack(parts)


def counter_of(c, group):
    out = jnp.zeros_like(c)
    for k, bit in enumerate(group):
        out = out + (((c >> (bit.bit_length() - 1)) & 1) << k)
    return out


def xor_sum(x, axis, size, radix_bits=2):
    if size & (size - 1):
        return lax.psum(x, axis)
    index = lax.axis_index(axis)
    bits = [1 << k for k in range(size.bit_length() - 1)][::-1]
    for group in [bits[i:i + radix_bits] for i in range(0, len(bits), radix_bits)]:
        mask = sum(group)
        stacked = xor_round(x, axis, size, group)
        order = [counter_of((v ^ (index & mask)), group) for v in range(mask + 1) if v & ~mask == 0]
        terms = [stacked[k] for k in order]
        while len(terms) > 1:
            terms = [terms[i] + terms[i + 1] for i in range(0, len(terms), 2)]
        x = terms[0]
    return x


def ordered_gather(block, owners, readers):
    reader_index = lax.axis_index("reader")
    owner_index = lax.axis_index("owner") if owners > 1 else 0
    group_size = readers // owners
    bits = [1 << k for k in range(readers.bit_length() - 1)][::-1]
    target = owner_index * group_size
    held = block[None]
    for group in bit_groups(bits):
        high = sum(bit for bit in group if bit >= group_size)
        low = [bit for bit in group if bit < group_size]
        stacked = xor_round(held, "reader", readers, group)
        c_high = (reader_index ^ target) & high
        picks = []
        values = sorted(sum(bit for k, bit in enumerate(low) if count >> k & 1) for count in range(1 << len(low)))
        for v in values:
            c = c_high + (v ^ (reader_index & sum(low)))
            picks.append(counter_of(c, group))
        chosen = jnp.take(stacked, jnp.stack(picks), axis=0)
        chosen = jnp.swapaxes(chosen, 0, 1)
        held = chosen.reshape((-1,) + block.shape)
    return held


def half_gather(block, owners, readers):
    held = ordered_gather(block, owners, readers)
    return jnp.transpose(held, (1, 0, 2)).reshape(block.shape[0], -1)


def local(acts, grads, basis_a, basis_g, eigvals, lengths, shuffle):
    owners = lax.axis_size("owner")
    readers = lax.axis_size("reader")
    owner_index = lax.axis_index("owner")
    rows = acts.shape[0] * readers
    slots = rows // SEQ
    m_block = basis_g.shape[0]
    n_block = basis_a.shape[0]
    width = eigvals.shape[1]
    dim_ff = m_block * readers
    dim_d = width * owners

    all_g = lax.all_gather(grads, "reader", axis=0, tiled=True)
    all_a = ordered_gather(acts, 1, readers).reshape(rows, acts.shape[1])

    token = jnp.arange(rows, dtype=jnp.int32)
    live = ((token % SEQ) < lengths[token // SEQ]).astype(jnp.float32)

    part_a = jnp.einsum("tk,jk->tj", all_a, basis_a, preferred_element_type=jnp.float32)
    rot_a_block = (xor_sum(part_a, "owner", owners) * live[:, None]).astype(jnp.bfloat16)
    pieces = []
    step = m_block // 2
    for start in range(0, m_block, step):
        part_g = jnp.einsum(
            "tk,jk->tj", all_g, basis_g[start:start + step], preferred_element_type=jnp.float32
        )
        pieces.append((xor_sum(part_g, "owner", owners) * live[:, None]).astype(jnp.bfloat16))
    rot_g = jnp.concatenate(pieces, axis=1)

    rot_a = half_gather(rot_a_block, owners, readers)

    denom = eigvals.astype(jnp.float32)
    g_rows = rot_g.reshape(slots, SEQ, m_block)
    a_rows = rot_a.reshape(slots, SEQ, width)
    outer = jnp.einsum("smt,smn->stn", g_rows, a_rows, preferred_element_type=jnp.float32)
    scaled = (outer / denom[None]).astype(jnp.bfloat16)
    projected = jnp.einsum("stm,smn->stn", g_rows, scaled, preferred_element_type=jnp.float32)
    partial = jnp.sum(projected * a_rows.astype(jnp.float32), axis=2) / (dim_ff * dim_d)
    scores = xor_sum(partial, ("owner", "reader"), owners * readers, radix_bits=3)

    token_score = lax.dynamic_index_in_dim(scores, owner_index, 0, keepdims=False)
    slot_mean = jnp.sum(scores, axis=1) / SEQ
    table = (shuffle[:, None] == jnp.arange(slots, dtype=jnp.int32)[None, :]).astype(jnp.float32)
    example_score = jnp.sum(slot_mean[:, None] * table, axis=0)
    return (token_score, example_score)


def solution(mesh):
    return jax.shard_map(
        local,
        mesh=mesh,
        in_specs=(
            P("reader", "owner"),
            P("reader", "owner"),
            P("reader", "owner"),
            P("reader", "owner"),
            P("reader", "owner"),
            P(),
            P(),
        ),
        out_specs=(P("owner"), P()),
        check_vma=False,
    )
```

```python
import jax
import jax.numpy as jnp
from jax import lax
from jax.sharding import PartitionSpec as P

SEQ = 128


def bit_groups(bits):
    return [bits[i:i + 2] for i in range(0, len(bits), 2)]


def xor_round(held, axis, size, group):
    parts = [held]
    for count in range(1, 1 << len(group)):
        c = sum(bit for k, bit in enumerate(group) if count >> k & 1)
        parts.append(lax.ppermute(held, axis, [(i, i ^ c) for i in range(size)]))
    return jnp.stack(parts)


def counter_of(c, group):
    out = jnp.zeros_like(c)
    for k, bit in enumerate(group):
        out = out + (((c >> (bit.bit_length() - 1)) & 1) << k)
    return out


def xor_sum(x, axis, size):
    if size & (size - 1):
        return lax.psum(x, axis)
    index = lax.axis_index(axis)
    bits = [1 << k for k in range(size.bit_length() - 1)][::-1]
    for group in bit_groups(bits):
        mask = sum(group)
        stacked = xor_round(x, axis, size, group)
        order = [counter_of((v ^ (index & mask)), group) for v in range(mask + 1) if v & ~mask == 0]
        terms = [stacked[k] for k in order]
        while len(terms) > 1:
            terms = [terms[i] + terms[i + 1] for i in range(0, len(terms), 2)]
        x = terms[0]
    return x


def ordered_gather(block, owners, readers, after=None):
    reader_index = lax.axis_index("reader")
    owner_index = lax.axis_index("owner") if owners > 1 else 0
    group_size = readers // owners
    bits = [1 << k for k in range(readers.bit_length() - 1)][::-1]
    target = owner_index * group_size
    held = block[None]
    groups = bit_groups(bits)
    for group in groups:
        high = sum(bit for bit in group if bit >= group_size)
        low = [bit for bit in group if bit < group_size]
        if after is not None and group is groups[-1]:
            held, _ = lax.optimization_barrier((held, after))
        stacked = xor_round(held, "reader", readers, group)
        c_high = (reader_index ^ target) & high
        picks = []
        values = sorted(sum(bit for k, bit in enumerate(low) if count >> k & 1) for count in range(1 << len(low)))
        for v in values:
            c = c_high + (v ^ (reader_index & sum(low)))
            picks.append(counter_of(c, group))
        chosen = jnp.take(stacked, jnp.stack(picks), axis=0)
        chosen = jnp.swapaxes(chosen, 0, 1)
        held = chosen.reshape((-1,) + block.shape)
    return held


def half_gather(block, owners, readers, after):
    held = ordered_gather(block, owners, readers, after)
    return jnp.transpose(held, (1, 0, 2)).reshape(block.shape[0], -1)


def local(acts, grads, basis_a, basis_g, eigvals, lengths, shuffle):
    owners = lax.axis_size("owner")
    readers = lax.axis_size("reader")
    owner_index = lax.axis_index("owner")
    rows = acts.shape[0] * readers
    slots = rows // SEQ
    m_block = basis_g.shape[0]
    n_block = basis_a.shape[0]
    width = eigvals.shape[1]
    dim_ff = m_block * readers
    dim_d = width * owners

    all_g = lax.all_gather(grads, "reader", axis=0, tiled=True)
    all_a = ordered_gather(acts, 1, readers).reshape(rows, acts.shape[1])

    token = jnp.arange(rows, dtype=jnp.int32)
    live = ((token % SEQ) < lengths[token // SEQ]).astype(jnp.float32)

    part_a = jnp.einsum("tk,jk->tj", all_a, basis_a, preferred_element_type=jnp.float32)
    rot_a_block = (xor_sum(part_a, "owner", owners) * live[:, None]).astype(jnp.bfloat16)
    first = m_block // 2
    parts_g = [
        jnp.einsum("tk,jk->tj", all_g, basis_g[start:stop], preferred_element_type=jnp.float32)
        for start, stop in ((0, first), (first, m_block))
    ]
    parts_g[0], eig_after = lax.optimization_barrier((parts_g[0], eigvals))
    pieces = [(xor_sum(part_g, "owner", owners) * live[:, None]).astype(jnp.bfloat16) for part_g in parts_g]
    rot_g = jnp.concatenate(pieces, axis=1)

    rot_a = half_gather(rot_a_block, owners, readers, parts_g[0])

    denom = eig_after.astype(jnp.float32)
    g_rows = rot_g.reshape(slots, SEQ, m_block)
    a_rows = rot_a.reshape(slots, SEQ, width)
    outer = jnp.einsum("smt,smn->stn", g_rows, a_rows, preferred_element_type=jnp.float32)
    scaled = (outer / denom[None]).astype(jnp.bfloat16)
    projected = jnp.einsum("stm,smn->stn", g_rows, scaled, preferred_element_type=jnp.float32)
    partial = jnp.sum(projected * a_rows.astype(jnp.float32), axis=2) / (dim_ff * dim_d)
    scores = xor_sum(xor_sum(partial, "reader", readers), "owner", owners)

    token_score = lax.dynamic_index_in_dim(scores, owner_index, 0, keepdims=False)
    slot_mean = jnp.sum(scores, axis=1) / SEQ
    table = (shuffle[:, None] == jnp.arange(slots, dtype=jnp.int32)[None, :]).astype(jnp.float32)
    example_score = jnp.sum(slot_mean[:, None] * table, axis=0)
    return (token_score, example_score)


def solution(mesh):
    return jax.shard_map(
        local,
        mesh=mesh,
        in_specs=(
            P("reader", "owner"),
            P("reader", "owner"),
            P("reader", "owner"),
            P("reader", "owner"),
            P("reader", "owner"),
            P(),
            P(),
        ),
        out_specs=(P("owner"), P()),
        check_vma=False,
    )
```

```python
import jax
import jax.numpy as jnp
from jax import lax
from jax.sharding import PartitionSpec as P

SEQ = 128


def bit_groups(bits):
    return [bits[i:i + 2] for i in range(0, len(bits), 2)]


def xor_round(held, axis, size, group):
    parts = [held]
    for count in range(1, 1 << len(group)):
        c = sum(bit for k, bit in enumerate(group) if count >> k & 1)
        parts.append(lax.ppermute(held, axis, [(i, i ^ c) for i in range(size)]))
    return jnp.stack(parts)


def counter_of(c, group):
    out = jnp.zeros_like(c)
    for k, bit in enumerate(group):
        out = out + (((c >> (bit.bit_length() - 1)) & 1) << k)
    return out


def xor_sum(x, axis, size):
    if size & (size - 1):
        return lax.psum(x, axis)
    index = lax.axis_index(axis)
    bits = [1 << k for k in range(size.bit_length() - 1)][::-1]
    for group in bit_groups(bits):
        mask = sum(group)
        stacked = xor_round(x, axis, size, group)
        order = [counter_of((v ^ (index & mask)), group) for v in range(mask + 1) if v & ~mask == 0]
        terms = [stacked[k] for k in order]
        while len(terms) > 1:
            terms = [terms[i] + terms[i + 1] for i in range(0, len(terms), 2)]
        x = terms[0]
    return x


def ordered_gather(block, owners, readers, after=None):
    reader_index = lax.axis_index("reader")
    owner_index = lax.axis_index("owner") if owners > 1 else 0
    group_size = readers // owners
    bits = [1 << k for k in range(readers.bit_length() - 1)][::-1]
    target = owner_index * group_size
    held = block[None]
    groups = bit_groups(bits)
    if after is not None:
        groups = groups[:-1] + [[bit] for bit in groups[-1]]
        gate_at = len(groups) - 2 if len(groups) > 1 and len(groups[-2]) == 1 else len(groups) - 1
    for step, group in enumerate(groups):
        high = sum(bit for bit in group if bit >= group_size)
        low = [bit for bit in group if bit < group_size]
        if after is not None and step == gate_at:
            held, _ = lax.optimization_barrier((held, after))
        stacked = xor_round(held, "reader", readers, group)
        c_high = (reader_index ^ target) & high
        picks = []
        values = sorted(sum(bit for k, bit in enumerate(low) if count >> k & 1) for count in range(1 << len(low)))
        for v in values:
            c = c_high + (v ^ (reader_index & sum(low)))
            picks.append(counter_of(c, group))
        chosen = jnp.take(stacked, jnp.stack(picks), axis=0)
        chosen = jnp.swapaxes(chosen, 0, 1)
        held = chosen.reshape((-1,) + block.shape)
    return held


def half_gather(block, owners, readers, after):
    held = ordered_gather(block, owners, readers, after)
    return jnp.transpose(held, (1, 0, 2)).reshape(block.shape[0], -1)


def local(acts, grads, basis_a, basis_g, eigvals, lengths, shuffle):
    owners = lax.axis_size("owner")
    readers = lax.axis_size("reader")
    owner_index = lax.axis_index("owner")
    rows = acts.shape[0] * readers
    slots = rows // SEQ
    m_block = basis_g.shape[0]
    n_block = basis_a.shape[0]
    width = eigvals.shape[1]
    dim_ff = m_block * readers
    dim_d = width * owners

    all_g = lax.all_gather(grads, "reader", axis=0, tiled=True)
    all_a = ordered_gather(acts, 1, readers).reshape(rows, acts.shape[1])

    token = jnp.arange(rows, dtype=jnp.int32)
    live = ((token % SEQ) < lengths[token // SEQ]).astype(jnp.float32)

    part_a = jnp.einsum("tk,jk->tj", all_a, basis_a, preferred_element_type=jnp.float32)
    rot_a_block = (xor_sum(part_a, "owner", owners) * live[:, None]).astype(jnp.bfloat16)
    first = m_block // 2
    parts_g = [
        jnp.einsum("tk,jk->tj", all_g, basis_g[start:stop], preferred_element_type=jnp.float32)
        for start, stop in ((0, first), (first, m_block))
    ]
    parts_g[0], eig_after = lax.optimization_barrier((parts_g[0], eigvals))
    pieces = [(xor_sum(part_g, "owner", owners) * live[:, None]).astype(jnp.bfloat16) for part_g in parts_g]
    rot_g = jnp.concatenate(pieces, axis=1)

    rot_a = half_gather(rot_a_block, owners, readers, parts_g[0])

    denom = eig_after.astype(jnp.float32)
    g_rows = rot_g.reshape(slots, SEQ, m_block)
    a_rows = rot_a.reshape(slots, SEQ, width)
    outer = jnp.einsum("smt,smn->stn", g_rows, a_rows, preferred_element_type=jnp.float32)
    scaled = (outer / denom[None]).astype(jnp.bfloat16)
    projected = jnp.einsum("stm,smn->stn", g_rows, scaled, preferred_element_type=jnp.float32)
    partial = jnp.sum(projected * a_rows.astype(jnp.float32), axis=2) / (dim_ff * dim_d)
    scores = xor_sum(xor_sum(partial, "reader", readers), "owner", owners)

    token_score = lax.dynamic_index_in_dim(scores, owner_index, 0, keepdims=False)
    slot_mean = jnp.sum(scores, axis=1) / SEQ
    table = (shuffle[:, None] == jnp.arange(slots, dtype=jnp.int32)[None, :]).astype(jnp.float32)
    example_score = jnp.sum(slot_mean[:, None] * table, axis=0)
    return (token_score, example_score)


def solution(mesh):
    return jax.shard_map(
        local,
        mesh=mesh,
        in_specs=(
            P("reader", "owner"),
            P("reader", "owner"),
            P("reader", "owner"),
            P("reader", "owner"),
            P("reader", "owner"),
            P(),
            P(),
        ),
        out_specs=(P("owner"), P()),
        check_vma=False,
    )
```
